512 devices in a mesh: chol: 32 (over y, z_hi, x), pair: 16 (over z_lo, core).
Axes of the slice: x: 4, y: 4, z: 16 (z_hi: 2, z_lo: 8; z = z_hi * 8 + z_lo), core: 2. Of those that a mesh axis runs over, the one named last changes fastest.
Arguments:
- rotated: float32 [16384, 32768], P('chol', 'pair'), may hold values from -0.03125 to 0.03125
- green: float32 [1024, 32768], P('chol', 'pair'), may hold values from -6 to 6
- aux_field: float32 [1024, 16384], P('pair', 'chol'), may hold values from -6 to 6
Outputs:
- shifted: float32 [1024, 16384], P('pair', 'chol')
The draws below stay inside these ranges and needn't reach their ends.
All inputs are finite; a program needn't handle non-finite values.
Results may differ from the reference program's by a relative error of at most 0.000056.
Values sent between devices are 32-bit elements; how exact they have to be, the bound alone decides.
No kernel may reach another device: no remote copies, remote signals or barrier semaphores. Data moves between devices by JAX's collectives and lax.ppermute only.
A program may use at most 64 MiB of HBM per device.

```python
import jax
import jax.numpy as jnp
from jax import lax

NCHOL = 16384
WALKERS = 1024
PAIRS = 32768


def with_spikes(drawn, stream_key, source, target, parts, factor):
    def block_of(axis_at):
        return (jnp.arange(drawn.shape[axis_at]) // (drawn.shape[axis_at] // parts)).reshape((-1,) + (1,) * (drawn.ndim - 1 - axis_at))

    near = jax.random.permutation(stream_key, parts)[block_of(target)]
    second = (block_of(target) + parts // 2) % parts
    return jnp.where((block_of(source) == near) | (block_of(source) == second), factor * drawn, drawn)


def steps_of(key, shape, split, least, high):
    gain = 1.0
    for axis_at, blocks in split:
        draws = jax.random.uniform(jax.random.fold_in(jax.random.fold_in(key, 6), axis_at), (blocks,), jnp.float32, least / len(split), high / len(split))
        gain = gain * jnp.repeat(jnp.exp(draws), shape[axis_at] // blocks).reshape((-1,) + (1,) * (len(shape) - 1 - axis_at))
    return gain


def gaussian(stream_key, extent, scale, reach, pieces=(), held_as=jnp.bfloat16):
    result = scale * jax.random.normal(stream_key, extent, jnp.float32)
    if pieces:
        result = result * steps_of(stream_key, extent, pieces, -0.22, 0.18)
    return jnp.clip(result, -reach, reach).astype(held_as)


def gaussian_with(key, shape, scale, limit, shards, heavy, held_as=jnp.bfloat16):
    values = scale * jax.random.normal(key, shape, jnp.float32)
    if shards:
        values = values * steps_of(key, shape, shards, -0.22, 0.18)
    return jnp.clip(with_spikes(values, jax.random.fold_in(key, 3), *heavy), -limit, limit).astype(held_as)


def setup_inputs(seed: int = 0) -> dict:
    key_list = jax.random.split(jax.random.key(seed), 4)
    return {
        "rotated": gaussian(key_list[0], (NCHOL, PAIRS), PAIRS ** -0.5, 0.03125, ((0, 32), (1, 16)), jnp.float32),
        "green": gaussian_with(key_list[1], (WALKERS, PAIRS), 1.0, 6.0, ((0, 32), (1, 16)), (1, 0, 32, 2.75), jnp.float32),
        "aux_field": gaussian(key_list[2], (WALKERS, NCHOL), 1.0, 6.0, ((0, 16), (1, 32)), jnp.float32),
    }


bias_cap = 1.5


def reference(rotated, green, aux_field):
    bias = lax.dot_general(green, rotated, (((1,), (1,)), ((), ())), precision=lax.Precision.HIGHEST, preferred_element_type=jnp.float32)
    capped = jnp.clip(bias, -bias_cap, bias_cap)
    return aux_field - capped
```

```python
import jax
import jax.numpy as jnp
from jax import lax
from jax.sharding import Mesh, PartitionSpec as P

bias_cap = 1.5
CHOL = ("y", "zh", "x")
PAIR = ("zl", "core")


def contract(rows, rotated):
    return lax.dot_general(rows, rotated, (((1,), (1,)), ((), ())),
                           precision=lax.Precision.HIGHEST, preferred_element_type=jnp.float32)


def body(rotated, green, aux_field):
    ny, nx = lax.axis_size("y"), lax.axis_size("x")
    nz = lax.axis_size("zh")
    rows = green.shape[0]
    g = lax.all_gather(green, "zh", axis=0, tiled=True)
    g = lax.all_gather(g, ("y", "x"), axis=0, tiled=True)
    part = contract(g, rotated)
    nl, nc = lax.axis_size("zl"), lax.axis_size("core")
    part = part.reshape(ny, nx, nz, rows, -1).transpose(0, 2, 1, 3, 4)
    part = part.reshape(nl, nc, -1, part.shape[-1]).transpose(1, 0, 2, 3).reshape(ny * nx * nz * rows, -1)
    share = lax.psum_scatter(part, "core", scatter_dimension=0, tiled=True)
    share = lax.psum_scatter(share, "zl", scatter_dimension=0, tiled=True)
    return aux_field - jnp.clip(share, -bias_cap, bias_cap)


def solution(mesh):
    ny, nz, nx = 4, 2, 4
    devs = mesh.devices.reshape(ny, nz, nx, mesh.devices.shape[1] // 2, 2)
    fine = Mesh(devs, CHOL + PAIR)
    placed = (P(CHOL, PAIR), P(CHOL, PAIR), P(PAIR, CHOL))
    return jax.shard_map(body, mesh=fine, in_specs=placed, out_specs=P(PAIR, CHOL), check_vma=False)
```

```python
import jax
import jax.numpy as jnp
from jax import lax
from jax.sharding import Mesh, PartitionSpec as P

bias_cap = 1.5
CHOL = ("y", "zh", "x")
PAIR = ("zl", "core")
SPLIT = False


def contract(rows, rotated):
    return lax.dot_general(rows, rotated, (((1,), (1,)), ((), ())),
                           precision=lax.Precision.HIGHEST, preferred_element_type=jnp.float32)


def swap(v, axis, bit):
    n = lax.axis_size(axis)
    return lax.ppermute(v, axis, [(i, i ^ bit) for i in range(n)])


def halve(m, axis, bit, at):
    mine = (lax.axis_index(axis) // bit) % 2
    keep = lax.dynamic_index_in_dim(m, mine, at, keepdims=False)
    send = lax.dynamic_index_in_dim(m, 1 - mine, at, keepdims=False)
    return keep + swap(send, axis, bit)


def reduce_scatter(part, nl, nc):
    m = part.reshape(nl, nc, -1, part.shape[-1])
    m = halve(m, "core", 1, 1)
    b = 1
    while b < nl:
        m = m.reshape(m.shape[0] // 2, 2, *m.shape[1:])
        m = halve(m, "zl", b, 1)
        b *= 2
    return m[0]


def body(rotated, green, aux_field):
    ny, nx, nz = lax.axis_size("y"), lax.axis_size("x"), lax.axis_size("zh")
    nl, nc = lax.axis_size("zl"), lax.axis_size("core")
    rows = green.shape[0]
    partner = swap(green, "zh", 1)
    first = lax.axis_index("zh") == 0
    if SPLIT:
        own = contract(lax.all_gather(green, ("y", "x"), axis=0, tiled=True), rotated)
        other = contract(lax.all_gather(partner, ("y", "x"), axis=0, tiled=True), rotated)
        own = own.reshape(ny, nx, rows, -1)
        other = other.reshape(ny, nx, rows, -1)
        part = jnp.stack([jnp.where(first, own, other), jnp.where(first, other, own)], axis=1)
    else:
        g = jnp.stack([jnp.where(first, green, partner), jnp.where(first, partner, green)])
        g = lax.all_gather(g, ("y", "x"), axis=0, tiled=True)
        part = contract(g.reshape(-1, g.shape[-1]), rotated)
        part = part.reshape(ny, nx, nz, rows, -1).transpose(0, 2, 1, 3, 4)
    part = part.reshape(ny * nz * nx * rows, -1)
    share = reduce_scatter(part, nl, nc)
    return aux_field - jnp.clip(share, -bias_cap, bias_cap)


def solution(mesh):
    ny, nz, nx = 4, 2, 4
    devs = mesh.devices.reshape(ny, nz, nx, mesh.devices.shape[1] // 2, 2)
    fine = Mesh(devs, CHOL + PAIR)
    placed = (P(CHOL, PAIR), P(CHOL, PAIR), P(PAIR, CHOL))
    return jax.shard_map(body, mesh=fine, in_specs=placed, out_specs=P(PAIR, CHOL), check_vma=False)
```

```python
import jax
import jax.numpy as jnp
from jax import lax
from jax.sharding import Mesh, PartitionSpec as P

bias_cap = 1.5
CHOL = ("y", "zh", "x")
PAIR = ("zl", "core")
SPLIT = False


def contract(rows, rotated):
    return lax.dot_general(rows, rotated, (((1,), (1,)), ((), ())),
                           precision=lax.Precision.HIGHEST, preferred_element_type=jnp.float32)


def shift(v, axis, k):
    n = lax.axis_size(axis)
    return lax.ppermute(v, axis, [(i, (i + k) % n) for i in range(n)])


def ring(v, axis):
    n = lax.axis_size(axis)
    got = {0: v}
    f = b = v
    for s in range(1, (n - 1) // 2 + 1):
        f = shift(f, axis, 1)
        got[n - s] = f
        b = shift(b, axis, -1)
        got[s] = b
    if n % 2 == 0:
        h = v.shape[-2] // 2
        lo = shift(f[..., :h, :], axis, 1)
        hi = shift(b[..., h:, :], axis, -1)
        got[n // 2] = jnp.concatenate([lo, hi], axis=-2)
    return jnp.stack([got[k] for k in range(n)])


def swap(v, axis, bit):
    n = lax.axis_size(axis)
    return lax.ppermute(v, axis, [(i, i ^ bit) for i in range(n)])


def halve(m, axis, bit, at):
    mine = (lax.axis_index(axis) // bit) % 2
    keep = lax.dynamic_index_in_dim(m, mine, at, keepdims=False)
    send = lax.dynamic_index_in_dim(m, 1 - mine, at, keepdims=False)
    return keep + swap(send, axis, bit)


def reduce_scatter(part, nl, nc):
    m = part.reshape(nl, nc, -1, part.shape[-1])
    m = halve(m, "core", 1, 1)
    b = 1
    while b < nl:
        m = m.reshape(m.shape[0] // 2, 2, *m.shape[1:])
        m = halve(m, "zl", b, 1)
        b *= 2
    return m[0]


def body(rotated, green, aux_field):
    ny, nx, nz = lax.axis_size("y"), lax.axis_size("x"), lax.axis_size("zh")
    nl, nc = lax.axis_size("zl"), lax.axis_size("core")
    rows = green.shape[0]
    partner = swap(green, "zh", 1)
    first = lax.axis_index("zh") == 0
    g = jnp.stack([jnp.where(first, green, partner), jnp.where(first, partner, green)])
    h = rows // 2

    def mm(t):
        return contract(t.reshape(-1, t.shape[-1]), rotated).reshape(t.shape[:-1] + (rotated.shape[0],))

    v1 = ring(ring(g[:, :h], "x"), "y")
    v2 = ring(ring(g[:, h:], "y"), "x")
    o = jnp.concatenate([mm(v1), mm(v2).transpose(1, 0, 2, 3, 4)], axis=3)
    o = jnp.roll(o, lax.axis_index("y"), axis=0)
    o = jnp.roll(o, lax.axis_index("x"), axis=1)
    part = o.transpose(0, 2, 1, 3, 4)
    part = part.reshape(ny * nz * nx * rows, -1)
    share = reduce_scatter(part, nl, nc)
    return aux_field - jnp.clip(share, -bias_cap, bias_cap)


def solution(mesh):
    ny, nz, nx = 4, 2, 4
    devs = mesh.devices.reshape(ny, nz, nx, mesh.devices.shape[1] // 2, 2)
    fine = Mesh(devs, CHOL + PAIR)
    placed = (P(CHOL, PAIR), P(CHOL, PAIR), P(PAIR, CHOL))
    return jax.shard_map(body, mesh=fine, in_specs=placed, out_specs=P(PAIR, CHOL), check_vma=False)
```

```python
import jax
import jax.numpy as jnp
from jax import lax
from jax.sharding import Mesh, PartitionSpec as P

bias_cap = 1.5
CHOL = ("y", "zh", "x")
PAIR = ("zl", "core")
SPLIT = False


def contract(rows, rotated):
    return lax.dot_general(rows, rotated, (((1,), (1,)), ((), ())),
                           precision=lax.Precision.HIGH, preferred_element_type=jnp.float32)


def shift(v, axis, k):
    n = lax.axis_size(axis)
    return lax.ppermute(v, axis, [(i, (i + k) % n) for i in range(n)])


def ring(v, axis):
    n = lax.axis_size(axis)
    got = {0: v}
    f = b = v
    for s in range(1, (n - 1) // 2 + 1):
        f = shift(f, axis, 1)
        got[n - s] = f
        b = shift(b, axis, -1)
        got[s] = b
    if n % 2 == 0:
        h = v.shape[-2] // 2
        lo = shift(f[..., :h, :], axis, 1)
        hi = shift(b[..., h:, :], axis, -1)
        got[n // 2] = jnp.concatenate([lo, hi], axis=-2)
    return jnp.stack([got[k] for k in range(n)])


def swap(v, axis, bit):
    n = lax.axis_size(axis)
    return lax.ppermute(v, axis, [(i, i ^ bit) for i in range(n)])


def halve(m, axis, bit, at):
    mine = (lax.axis_index(axis) // bit) % 2
    keep = lax.dynamic_index_in_dim(m, mine, at, keepdims=False)
    send = lax.dynamic_index_in_dim(m, 1 - mine, at, keepdims=False)
    return keep + swap(send, axis, bit)


def reduce_scatter(part, nl, nc):
    m = part.reshape(nl, nc, -1, part.shape[-1])
    m = halve(m, "core", 1, 1)
    b = 1
    while b < nl:
        m = m.reshape(m.shape[0] // 2, 2, *m.shape[1:])
        m = halve(m, "zl", b, 1)
        b *= 2
    return m[0]


def body(rotated, green, aux_field):
    ny, nx, nz = lax.axis_size("y"), lax.axis_size("x"), lax.axis_size("zh")
    nl, nc = lax.axis_size("zl"), lax.axis_size("core")
    rows = green.shape[0]
    partner = swap(green, "zh", 1)
    first = lax.axis_index("zh") == 0
    g = jnp.stack([jnp.where(first, green, partner), jnp.where(first, partner, green)])
    h = rows // 2

    def mm(t):
        return contract(t.reshape(-1, t.shape[-1]), rotated).reshape(t.shape[:-1] + (rotated.shape[0],))

    v1 = ring(ring(g[:, :h], "x"), "y")
    v2 = ring(ring(g[:, h:], "y"), "x")
    o = jnp.concatenate([mm(v1), mm(v2).transpose(1, 0, 2, 3, 4)], axis=3)
    o = jnp.roll(o, lax.axis_index("y"), axis=0)
    o = jnp.roll(o, lax.axis_index("x"), axis=1)
    part = o.transpose(0, 2, 1, 3, 4)
    part = part.reshape(ny * nz * nx * rows, -1)
    share = reduce_scatter(part, nl, nc)
    return aux_field - jnp.clip(share, -bias_cap, bias_cap)


def solution(mesh):
    ny, nz, nx = 4, 2, 4
    devs = mesh.devices.reshape(ny, nz, nx, mesh.devices.shape[1] // 2, 2)
    fine = Mesh(devs, CHOL + PAIR)
    placed = (P(CHOL, PAIR), P(CHOL, PAIR), P(PAIR, CHOL))
    return jax.shard_map(body, mesh=fine, in_specs=placed, out_specs=P(PAIR, CHOL), check_vma=False)
```

```python
import jax
import jax.numpy as jnp
from jax import lax
from jax.sharding import Mesh, PartitionSpec as P

bias_cap = 1.5
CHOL = ("y", "zh", "x")
PAIR = ("zl", "core")
SPLIT = False


def contract(rows, rotated):
    return lax.dot_general(rows, rotated, (((1,), (1,)), ((), ())),
                           precision=lax.Precision.HIGH, preferred_element_type=jnp.float32)


def shift(v, axis, k):
    n = lax.axis_size(axis)
    return lax.ppermute(v, axis, [(i, (i + k) % n) for i in range(n)])


def ring(v, axis):
    n = lax.axis_size(axis)
    got = {0: v}
    f = b = v
    for s in range(1, (n - 1) // 2 + 1):
        f = shift(f, axis, 1)
        got[n - s] = f
        b = shift(b, axis, -1)
        got[s] = b
    if n % 2 == 0:
        h = v.shape[-2] // 2
        lo = shift(f[..., :h, :], axis, 1)
        hi = shift(b[..., h:, :], axis, -1)
        got[n // 2] = jnp.concatenate([lo, hi], axis=-2)
    return jnp.stack([got[k] for k in range(n)])


def swap(v, axis, bit):
    n = lax.axis_size(axis)
    return lax.ppermute(v, axis, [(i, i ^ bit) for i in range(n)])


def halve(m, axis, bit, at):
    mine = (lax.axis_index(axis) // bit) % 2
    keep = lax.dynamic_index_in_dim(m, mine, at, keepdims=False)
    send = lax.dynamic_index_in_dim(m, 1 - mine, at, keepdims=False)
    return keep + swap(send, axis, bit)


def reduce_scatter(part, nl, nc):
    m = part.reshape(nl, nc, -1, part.shape[-1])
    m = halve(m, "core", 1, 1)
    b = 1
    while b < nl:
        m = m.reshape(m.shape[0] // 2, 2, *m.shape[1:])
        m = halve(m, "zl", b, 1)
        b *= 2
    return m[0]


def body(rotated, green, aux_field):
    ny, nx, nz = lax.axis_size("y"), lax.axis_size("x"), lax.axis_size("zh")
    nl, nc = lax.axis_size("zl"), lax.axis_size("core")
    rows = green.shape[0]
    partner = swap(green, "zh", 1)
    first = lax.axis_index("zh") == 0

    def mm(t):
        return contract(t.reshape(-1, t.shape[-1]), rotated).reshape(t.shape[:-1] + (rotated.shape[0],))

    own = mm(ring(ring(green, "x"), "y"))
    other = mm(ring(ring(partner, "y"), "x")).transpose(1, 0, 2, 3)
    o = jnp.roll(jnp.stack([own, other], axis=2), lax.axis_index("zh"), axis=2)
    o = jnp.roll(o, lax.axis_index("y"), axis=0)
    o = jnp.roll(o, lax.axis_index("x"), axis=1)
    part = o.transpose(0, 2, 1, 3, 4)
    part = part.reshape(ny * nz * nx * rows, -1)
    share = reduce_scatter(part, nl, nc)
    return aux_field - jnp.clip(share, -bias_cap, bias_cap)


def solution(mesh):
    ny, nz, nx = 4, 2, 4
    devs = mesh.devices.reshape(ny, nz, nx, mesh.devices.shape[1] // 2, 2)
    fine = Mesh(devs, CHOL + PAIR)
    placed = (P(CHOL, PAIR), P(CHOL, PAIR), P(PAIR, CHOL))
    return jax.shard_map(body, mesh=fine, in_specs=placed, out_specs=P(PAIR, CHOL), check_vma=False)
```

```python
import jax
import jax.numpy as jnp
from jax import lax
from jax.sharding import Mesh, PartitionSpec as P

bias_cap = 1.5
CHOL = ("y", "zh", "x")
PAIR = ("zl", "core")
SPLIT = False


def contract(rows, rotated):
    return lax.dot_general(rows, rotated, (((1,), (1,)), ((), ())),
                           precision=lax.Precision.HIGH, preferred_element_type=jnp.float32)


def shift(v, axis, k):
    n = lax.axis_size(axis)
    return lax.ppermute(v, axis, [(i, (i + k) % n) for i in range(n)])


def ring(v, axis, split=True):
    n = lax.axis_size(axis)
    got = {0: v}
    f = b = v
    for s in range(1, (n - 1) // 2 + 1):
        f = shift(f, axis, 1)
        got[n - s] = f
        b = shift(b, axis, -1)
        got[s] = b
    if n % 2 == 0 and not split:
        got[n // 2] = shift(f, axis, 1)
    elif n % 2 == 0:
        h = v.shape[-2] // 2
        lo = shift(f[..., :h, :], axis, 1)
        hi = shift(b[..., h:, :], axis, -1)
        got[n // 2] = jnp.concatenate([lo, hi], axis=-2)
    return jnp.stack([got[k] for k in range(n)])


def swap(v, axis, bit):
    n = lax.axis_size(axis)
    return lax.ppermute(v, axis, [(i, i ^ bit) for i in range(n)])


def halve(m, axis, bit, at):
    mine = (lax.axis_index(axis) // bit) % 2
    keep = lax.dynamic_index_in_dim(m, mine, at, keepdims=False)
    send = lax.dynamic_index_in_dim(m, 1 - mine, at, keepdims=False)
    return keep + swap(send, axis, bit)


def reduce_scatter(part, nl, nc):
    m = part.reshape(nl, nc, -1, part.shape[-1])
    m = halve(m, "core", 1, 1)
    b = 1
    while b < nl:
        m = m.reshape(m.shape[0] // 2, 2, *m.shape[1:])
        m = halve(m, "zl", b, 1)
        b *= 2
    return m[0]


def body(rotated, green, aux_field):
    ny, nx, nz = lax.axis_size("y"), lax.axis_size("x"), lax.axis_size("zh")
    nl, nc = lax.axis_size("zl"), lax.axis_size("core")
    rows = green.shape[0]
    partner = swap(green, "zh", 1)
    first = lax.axis_index("zh") == 0

    def mm(t):
        return contract(t.reshape(-1, t.shape[-1]), rotated).reshape(t.shape[:-1] + (rotated.shape[0],))

    own = mm(ring(ring(green, "x", split=False), "y"))
    other = mm(ring(ring(partner, "y", split=False), "x")).transpose(1, 0, 2, 3)
    o = jnp.roll(jnp.stack([own, other], axis=2), lax.axis_index("zh"), axis=2)
    o = jnp.roll(o, lax.axis_index("y"), axis=0)
    o = jnp.roll(o, lax.axis_index("x"), axis=1)
    part = o.transpose(0, 2, 1, 3, 4)
    part = part.reshape(ny * nz * nx * rows, -1)
    share = reduce_scatter(part, nl, nc)
    return aux_field - jnp.clip(share, -bias_cap, bias_cap)


def solution(mesh):
    ny, nz, nx = 4, 2, 4
    devs = mesh.devices.reshape(ny, nz, nx, mesh.devices.shape[1] // 2, 2)
    fine = Mesh(devs, CHOL + PAIR)
    placed = (P(CHOL, PAIR), P(CHOL, PAIR), P(PAIR, CHOL))
    return jax.shard_map(body, mesh=fine, in_specs=placed, out_specs=P(PAIR, CHOL), check_vma=False)
```
